1024 devices in a mesh: mp: 8 (over x_hi, y), replica: 128 (over z, x_lo, core).
Axes of the slice: x: 4 (x_hi: 2, x_lo: 2; x = x_hi * 2 + x_lo), y: 4, z: 32, core: 2. Of those that a mesh axis runs over, the one named last changes fastest.
Arguments:
- pre: bfloat16 [128, 128, 12288], P('replica', None, 'mp'), may hold values from -6 to 6
- tok_keys: int32 [128, 128], P('replica'), may hold values from 0 to 16777215
- cotangent: bfloat16 [128, 128, 3072], P('replica', 'mp'), may hold values from -6 to 6
- w_out: bfloat16 [12288, 3072], P('mp'), may hold values from -0.0546875 to 0.0546875
- unit_keys: int32 [12288], P('mp'), may hold values from 0 to 16777215
- drop_salt: int32 [1], replicated, may hold values from 0 to 1073741823
- layer_key: int32 [1], replicated, may hold values from 0 to 63
- patch_count: int32 [128], P('replica'), may hold values from 64 to 128, as said below
Outputs:
- grad_pre: bfloat16 [128, 128, 12288], P('replica', None, 'mp')
- grad_bias: float32 [12288], P('mp')
The draws below stay inside these ranges and needn't reach their ends.
Inputs may be any that keep to these rules, and one draw needn't show every extreme that they name: `patch_count`: at least one image uses all 128 patches.
All inputs are finite; a program needn't handle non-finite values.
Results may differ from the reference program's by a relative error of at most 0.007.
Values may be sent and summed in bfloat16 or wider, within the bound.
No kernel may reach another device: no remote copies, remote signals or barrier semaphores. Data moves between devices by JAX's collectives and lax.ppermute only.
A program may use at most 32 MiB of HBM per device.

```python
import jax
import jax.numpy as jnp
from jax import lax

D = 3072
PATCHES = 128
FF = 12288
IMAGES = 128


def draw_patch_count(key, part):
    first, second = jax.random.split(jax.random.fold_in(key, 17))
    counts = jax.random.randint(first, (IMAGES,), PATCHES // 2, PATCHES + 1, dtype=jnp.int32)
    chosen = jax.random.randint(second, (), 0, IMAGES, dtype=jnp.int32)
    return jnp.where(jnp.arange(IMAGES, dtype=jnp.int32) == chosen, jnp.int32(PATCHES), counts)


def plant(drawn, key, low, top_value):
    index_at = [jax.random.randint(jax.random.fold_in(key, axis), (), 0, length) for axis, length in enumerate(drawn.shape)]
    longest = drawn.shape.index(max(drawn.shape))
    neighbour = index_at[:longest] + [(index_at[longest] + 1) % drawn.shape[longest]] + index_at[longest + 1:]
    return drawn.at[tuple(index_at)].set(low).at[tuple(neighbour)].set(top_value)


def shard_levels(stream_key, extent, shards, low, largest):
    level = 1.0
    for dim, shards_of in shards:
        draws = jax.random.uniform(jax.random.fold_in(jax.random.fold_in(stream_key, 6), dim), (shards_of,), jnp.float32, low / len(shards), largest / len(shards))
        level = level * jnp.repeat(jnp.exp(draws), extent[dim] // shards_of).reshape((-1,) + (1,) * (len(extent) - 1 - dim))
    return level


def noise(key, shape, scale, reach, pieces=(), kind=jnp.bfloat16):
    values = jax.random.normal(key, shape, jnp.float32) * scale
    if len(pieces) > 0:
        values = shard_levels(key, shape, pieces, -0.22, 0.18) * values
    return jnp.clip(values, min=-reach, max=reach).astype(kind)


def setup_inputs(seed: int = 0) -> dict:
    seeds = jax.random.split(jax.random.key(seed), 9)
    pre = noise(seeds[0], (IMAGES, PATCHES, FF), 1.5, 6.0, ((0, 128), (2, 8)))
    tok_keys = plant(jax.random.randint(seeds[1], (IMAGES, PATCHES), 0, 16777216), jax.random.fold_in(seeds[1], 1), 0, 16777215).astype(jnp.int32)
    cotangent = noise(seeds[2], (IMAGES, PATCHES, D), 1.0, 6.0, ((0, 128), (1, 8)))
    w_out = noise(seeds[3], (FF, D), FF ** -0.5, 0.0546875, ((0, 8),))
    unit_keys = plant(jax.random.randint(seeds[4], (FF,), 0, 16777216), jax.random.fold_in(seeds[4], 1), 0, 16777215).astype(jnp.int32)
    drop_salt = jax.random.randint(seeds[5], (1,), 0, 1073741824).astype(jnp.int32)
    layer_key = jax.random.randint(seeds[6], (1,), 0, 64).astype(jnp.int32)
    patch_count = draw_patch_count(jax.random.fold_in(seeds[8], 71), 0)
    return {"pre": pre, "tok_keys": tok_keys, "cotangent": cotangent, "w_out": w_out, "unit_keys": unit_keys, "drop_salt": drop_salt, "layer_key": layer_key, "patch_count": patch_count}


keep_scale = 1.0 / 0.9

def scramble(value):
    value = value * jnp.int32(73244475)
    return value ^ lax.shift_right_logical(value, jnp.int32(16))

def mixing(value):
    return scramble(scramble(value))

def drop_scale(salt_value, layer_value, tok_row, unit_row):
    base = mixing(salt_value * jnp.int32(1103515245) + layer_value)
    row_code = mixing(base ^ tok_row)
    code = mixing(row_code[:, None] + unit_row[None, :] * jnp.int32(40503))
    return jnp.where(code & jnp.int32(65535) >= jnp.int32(6554), jnp.float32(keep_scale), jnp.float32(0.0))

def gelu_tanh(value):
    return jax.nn.gelu(value, approximate=True)

def reference(pre, tok_keys, cotangent, w_out, unit_keys, drop_salt, layer_key, patch_count):

    def per_image(carry, item):
        pre_rows, keys_row, cot_rows, count = item
        scale = drop_scale(drop_salt[0], layer_key[0], keys_row, unit_keys)
        valid = jnp.arange(PATCHES, dtype=jnp.int32) < count
        masked = jnp.where(valid[:, None], cot_rows, jnp.zeros_like(cot_rows))
        dhid = jnp.dot(masked, w_out.T, preferred_element_type=jnp.float32)
        _, gelu_back = jax.vjp(gelu_tanh, pre_rows.astype(jnp.float32))
        grad_rows = gelu_back(dhid * scale)[0].astype(jnp.bfloat16)
        term = lax.optimization_barrier(jnp.sum(grad_rows.astype(jnp.float32), axis=0))
        return (carry + term, grad_rows)
    start = jnp.zeros((FF,), jnp.float32)
    total, grad_pre = lax.scan(per_image, start, (pre, tok_keys, cotangent, patch_count))
    return (grad_pre, total / jnp.float32(IMAGES))
```

```python
import jax
import jax.numpy as jnp
from jax import lax
from jax.sharding import Mesh, PartitionSpec as P

keep_scale = 1.0 / 0.9


def scramble(value):
    value = value * jnp.int32(73244475)
    return value ^ lax.shift_right_logical(value, jnp.int32(16))


def mixing(value):
    return scramble(scramble(value))


def drop_scale(salt_value, layer_value, tok_row, unit_row):
    base = mixing(salt_value * jnp.int32(1103515245) + layer_value)
    row_code = mixing(base ^ tok_row)
    code = mixing(row_code[:, None] + unit_row[None, :] * jnp.int32(40503))
    return jnp.where(
        code & jnp.int32(65535) >= jnp.int32(6554), jnp.float32(keep_scale), jnp.float32(0.0)
    )


def gelu_tanh(value):
    return jax.nn.gelu(value, approximate=True)


MP = ("xh", "y")
REP = ("z", "xl", "c")


def per_device(pre, tok_keys, cotangent, w_out, unit_keys, drop_salt, layer_key, patch_count):
    local_rows = cotangent.shape[1]
    patches = pre.shape[1]
    units = w_out.shape[0]
    groups = patches // local_rows
    replicas = lax.axis_size(REP)
    positions = lax.axis_index(MP) * local_rows + jnp.arange(local_rows, dtype=jnp.int32)
    valid = positions < patch_count[0]
    masked = jnp.where(valid[:, None], cotangent[0], jnp.zeros_like(cotangent[0]))
    gathered = lax.all_to_all(
        jnp.broadcast_to(masked[None], (groups,) + masked.shape), MP, 0, 0, tiled=True
    ).reshape(patches, masked.shape[1])
    scale = drop_scale(drop_salt[0], layer_key[0], tok_keys[0], unit_keys)
    pre_full = pre[0].astype(jnp.float32)
    part = lax.dot_general(
        gathered,
        w_out,
        (((1,), (1,)), ((), ())),
        preferred_element_type=jnp.float32,
    )
    _, gelu_back = jax.vjp(gelu_tanh, pre_full)
    grad_pre = gelu_back(part * scale)[0].astype(jnp.bfloat16)
    term = jnp.sum(grad_pre.astype(jnp.float32), axis=0)
    total = lax.psum(term, ("xl", "c"))
    total = lax.psum(total, "z")
    return (grad_pre.reshape(1, patches, units), total / jnp.float32(replicas))


def solution(mesh):
    mp, replica = mesh.shape["mp"], mesh.shape["replica"]
    fine = Mesh(
        mesh.devices.reshape(2, mp // 2, replica // 4, 2, 2), MP + REP
    )
    return jax.shard_map(
        per_device,
        mesh=fine,
        in_specs=(
            P(REP, None, MP),
            P(REP, None),
            P(REP, MP, None),
            P(MP, None),
            P(MP),
            P(),
            P(),
            P(REP),
        ),
        out_specs=(P(REP, None, MP), P(MP)),
        check_vma=False,
    )
```

```python
import jax
import jax.numpy as jnp
from jax import lax
from jax.sharding import Mesh, PartitionSpec as P

keep_scale = 1.0 / 0.9


def scramble(value):
    value = value * jnp.int32(73244475)
    return value ^ lax.shift_right_logical(value, jnp.int32(16))


def mixing(value):
    return scramble(scramble(value))


def drop_scale(salt_value, layer_value, tok_row, unit_row):
    base = mixing(salt_value * jnp.int32(1103515245) + layer_value)
    row_code = mixing(base ^ tok_row)
    code = mixing(row_code[:, None] + unit_row[None, :] * jnp.int32(40503))
    return jnp.where(
        code & jnp.int32(65535) >= jnp.int32(6554), jnp.float32(keep_scale), jnp.float32(0.0)
    )


def gelu_tanh(value):
    return jax.nn.gelu(value, approximate=True)


MP = ("xh", "y")
REP = ("zh", "zl", "xl", "c")


def per_device(pre, tok_keys, cotangent, w_out, unit_keys, drop_salt, layer_key, patch_count):
    local_rows = cotangent.shape[1]
    patches = pre.shape[1]
    units = w_out.shape[0]
    groups = patches // local_rows
    replicas = lax.axis_size(REP)
    positions = lax.axis_index(MP) * local_rows + jnp.arange(local_rows, dtype=jnp.int32)
    valid = positions < patch_count[0]
    masked = jnp.where(valid[:, None], cotangent[0], jnp.zeros_like(cotangent[0]))
    gathered = lax.all_to_all(
        jnp.broadcast_to(masked[None], (groups,) + masked.shape), MP, 0, 0, tiled=True
    ).reshape(patches, masked.shape[1])
    scale = drop_scale(drop_salt[0], layer_key[0], tok_keys[0], unit_keys)
    pre_full = pre[0].astype(jnp.float32)
    part = lax.dot_general(
        gathered,
        w_out,
        (((1,), (1,)), ((), ())),
        preferred_element_type=jnp.float32,
    )
    _, gelu_back = jax.vjp(gelu_tanh, pre_full)
    grad_pre = gelu_back(part * scale)[0].astype(jnp.bfloat16)
    term = jnp.sum(grad_pre.astype(jnp.float32), axis=0)
    total = lax.psum(term, ("xl", "c"))
    total = lax.psum(total, "zl")
    total = lax.psum(total, "zh")
    return (grad_pre.reshape(1, patches, units), total / jnp.float32(replicas))


def solution(mesh):
    mp, replica = mesh.shape["mp"], mesh.shape["replica"]
    fine = Mesh(
        mesh.devices.reshape(2, mp // 2, replica // 16, 4, 2, 2), MP + REP
    )
    return jax.shard_map(
        per_device,
        mesh=fine,
        in_specs=(
            P(REP, None, MP),
            P(REP, None),
            P(REP, MP, None),
            P(MP, None),
            P(MP),
            P(),
            P(),
            P(REP),
        ),
        out_specs=(P(REP, None, MP), P(MP)),
        check_vma=False,
    )
```

```python
import jax
import jax.numpy as jnp
from jax import lax
from jax.sharding import Mesh, PartitionSpec as P

keep_scale = 1.0 / 0.9


def scramble(value):
    value = value * jnp.int32(73244475)
    return value ^ lax.shift_right_logical(value, jnp.int32(16))


def mixing(value):
    return scramble(scramble(value))


def drop_scale(salt_value, layer_value, tok_row, unit_row):
    base = mixing(salt_value * jnp.int32(1103515245) + layer_value)
    row_code = mixing(base ^ tok_row)
    code = mixing(row_code[:, None] + unit_row[None, :] * jnp.int32(40503))
    return jnp.where(
        code & jnp.int32(65535) >= jnp.int32(6554), jnp.float32(keep_scale), jnp.float32(0.0)
    )


def gelu_tanh(value):
    return jax.nn.gelu(value, approximate=True)


MP = ("xh", "y")
REP = ("zh", "zm", "zl", "xl", "c")


def per_device(pre, tok_keys, cotangent, w_out, unit_keys, drop_salt, layer_key, patch_count):
    local_rows = cotangent.shape[1]
    patches = pre.shape[1]
    units = w_out.shape[0]
    groups = patches // local_rows
    replicas = lax.axis_size(REP)
    positions = lax.axis_index(MP) * local_rows + jnp.arange(local_rows, dtype=jnp.int32)
    valid = positions < patch_count[0]
    masked = jnp.where(valid[:, None], cotangent[0], jnp.zeros_like(cotangent[0]))
    gathered = lax.all_to_all(
        jnp.broadcast_to(masked[None], (groups,) + masked.shape), MP, 0, 0, tiled=True
    ).reshape(patches, masked.shape[1])
    scale = drop_scale(drop_salt[0], layer_key[0], tok_keys[0], unit_keys)
    pre_full = pre[0].astype(jnp.float32)
    part = lax.dot_general(
        gathered,
        w_out,
        (((1,), (1,)), ((), ())),
        preferred_element_type=jnp.float32,
    )
    _, gelu_back = jax.vjp(gelu_tanh, pre_full)
    grad_pre = gelu_back(part * scale)[0].astype(jnp.bfloat16)
    term = jnp.sum(grad_pre.astype(jnp.float32), axis=0)
    total = lax.psum(term, ("xl", "c"))
    total = lax.psum(total, "zl")
    total = lax.psum(total, "zm")
    total = lax.psum(total, "zh")
    return (grad_pre.reshape(1, patches, units), total / jnp.float32(replicas))


def solution(mesh):
    mp, replica = mesh.shape["mp"], mesh.shape["replica"]
    fine = Mesh(
        mesh.devices.reshape(2, mp // 2, replica // 32, 2, 4, 2, 2), MP + REP
    )
    return jax.shard_map(
        per_device,
        mesh=fine,
        in_specs=(
            P(REP, None, MP),
            P(REP, None),
            P(REP, MP, None),
            P(MP, None),
            P(MP),
            P(),
            P(),
            P(REP),
        ),
        out_specs=(P(REP, None, MP), P(MP)),
        check_vma=False,
    )
```

```python
import jax
import jax.numpy as jnp
from jax import lax
from jax.sharding import Mesh, PartitionSpec as P

keep_scale = 1.0 / 0.9


def scramble(value):
    value = value * jnp.int32(73244475)
    return value ^ lax.shift_right_logical(value, jnp.int32(16))


def mixing(value):
    return scramble(scramble(value))


def drop_scale(salt_value, layer_value, tok_row, unit_row):
    base = mixing(salt_value * jnp.int32(1103515245) + layer_value)
    row_code = mixing(base ^ tok_row)
    code = mixing(row_code[:, None] + unit_row[None, :] * jnp.int32(40503))
    return jnp.where(
        code & jnp.int32(65535) >= jnp.int32(6554), jnp.float32(keep_scale), jnp.float32(0.0)
    )


def gelu_tanh(value):
    return jax.nn.gelu(value, approximate=True)


MP = ("xh", "y")
REP = ("zh", "zl", "xl", "c")


def per_device(pre, tok_keys, cotangent, w_out, unit_keys, drop_salt, layer_key, patch_count):
    local_rows = cotangent.shape[1]
    patches = pre.shape[1]
    units = w_out.shape[0]
    groups = patches // local_rows
    replicas = lax.axis_size(REP)
    positions = lax.axis_index(MP) * local_rows + jnp.arange(local_rows, dtype=jnp.int32)
    valid = positions < patch_count[0]
    masked = jnp.where(valid[:, None], cotangent[0], jnp.zeros_like(cotangent[0]))
    gathered = lax.all_to_all(
        jnp.broadcast_to(masked[None], (groups,) + masked.shape), MP, 0, 0, tiled=True
    ).reshape(patches, masked.shape[1])
    scale = drop_scale(drop_salt[0], layer_key[0], tok_keys[0], unit_keys)
    pre_full = pre[0].astype(jnp.float32)
    part = lax.dot_general(
        gathered,
        w_out,
        (((1,), (1,)), ((), ())),
        preferred_element_type=jnp.float32,
    )
    _, gelu_back = jax.vjp(gelu_tanh, pre_full)
    factor = lax.optimization_barrier(gelu_back(scale)[0])
    grad_pre = (part * factor).astype(jnp.bfloat16)
    term = jnp.sum(grad_pre.astype(jnp.float32), axis=0)
    total = lax.psum(term, ("xl", "c"))
    total = lax.psum(total, "zl")
    total = lax.psum(total, "zh")
    return (grad_pre.reshape(1, patches, units), total / jnp.float32(replicas))


def solution(mesh):
    mp, replica = mesh.shape["mp"], mesh.shape["replica"]
    fine = Mesh(
        mesh.devices.reshape(2, mp // 2, replica // 16, 4, 2, 2), MP + REP
    )
    return jax.shard_map(
        per_device,
        mesh=fine,
        in_specs=(
            P(REP, None, MP),
            P(REP, None),
            P(REP, MP, None),
            P(MP, None),
            P(MP),
            P(),
            P(),
            P(REP),
        ),
        out_specs=(P(REP, None, MP), P(MP)),
        check_vma=False,
    )
```
